256 devices in a mesh: seq: 32 (over z_hi, y, x), wt: 2 (over core), head: 4 (over z_lo).
Axes of the slice: x: 4, y: 4, z: 8 (z_hi: 2, z_lo: 4; z = z_hi * 4 + z_lo), core: 2. Of those that a mesh axis runs over, the one named last changes fastest.
Arguments:
- tokens: bfloat16 [2, 4096, 5120], P('wt', 'seq'), may hold values from -6 to 6
- w_query: bfloat16 [5120, 2560], P('wt', 'head'), may hold values from -0.078125 to 0.078125
- w_key: bfloat16 [5120, 2560], P('wt', 'head'), may hold values from -0.078125 to 0.078125
- w_value: bfloat16 [5120, 2560], P('wt', 'head'), may hold values from -0.078125 to 0.078125
- w_output: bfloat16 [2560, 5120], P('head', 'wt'), may hold values from -0.125 to 0.125
Outputs:
- mixed: bfloat16 [2, 4096, 5120], P('wt', 'seq', 'head')
The draws below stay inside these ranges and needn't reach their ends.
All inputs are finite; a program needn't handle non-finite values.
Results may differ from the reference program's by a relative error of at most 0.013.
Values may be sent and summed in bfloat16 or wider, within the bound.
No kernel may reach another device: no remote copies, remote signals or barrier semaphores. Data moves between devices by JAX's collectives and lax.ppermute only.
A program may use at most 128 MiB of HBM per device.

```python
import jax
import jax.numpy as jnp
from jax import lax

D = 5120
HD = 128
HEADS = 20
TOK_DEV = 128
LENGTH = 4096
BATCH = 2


def steps_of(rng, dims, cuts, low, high):
    gain, own = 1.0, jax.random.fold_in(rng, 6)
    for dim, parts in cuts:
        steps = jnp.exp(jax.random.uniform(jax.random.fold_in(own, dim), (parts,), jnp.float32, low / len(cuts), high / len(cuts)))
        gain = gain * jnp.repeat(steps, dims[dim] // parts).reshape([-1 if axis == dim else 1 for axis in range(len(dims))])
    return gain


def scatter_about(rng, extent, deviation, reach, shards=(), held_as=jnp.bfloat16):
    drawn = jax.random.normal(rng, extent, jnp.float32) * deviation
    if len(shards) > 0:
        drawn = steps_of(rng, extent, shards, -0.22, 0.18) * drawn
    return jnp.clip(drawn, min=-reach, max=reach).astype(held_as)


def setup_inputs(seed: int = 0) -> dict:
    streams_of = jax.random.split(jax.random.key(seed), 6)
    return {
        "tokens": scatter_about(streams_of[0], (BATCH, LENGTH, D), 1.0, 6.0, ((0, 2), (1, 32))),
        "w_query": scatter_about(streams_of[1], (D, HEADS * HD), D ** -0.5, 0.078125, ((0, 2), (1, 4))),
        "w_key": scatter_about(streams_of[2], (D, HEADS * HD), D ** -0.5, 0.078125, ((0, 2), (1, 4))),
        "w_value": scatter_about(streams_of[3], (D, HEADS * HD), D ** -0.5, 0.078125, ((0, 2), (1, 4))),
        "w_output": scatter_about(streams_of[4], (HEADS * HD, D), (HEADS * HD) ** -0.5, 0.125, ((0, 4), (1, 2))),
    }


def attend_block(prefix_state, block):
    queries, keys, values = block
    scores = jnp.einsum('thd,shd->hts', queries, keys, preferred_element_type=jnp.float32)
    rows = jnp.arange(queries.shape[0])
    causal = (rows[None, :] <= rows[:, None]).astype(jnp.float32)
    scores = (scores * causal[None, :, :]).astype(jnp.bfloat16)
    local_part = jnp.einsum('hts,shd->thd', scores, values, preferred_element_type=jnp.float32)
    carried = jnp.einsum('thd,hde->the', queries.astype(jnp.float32), prefix_state, precision=lax.Precision.HIGHEST)
    block_state = jnp.einsum('thd,the->hde', keys, values, preferred_element_type=jnp.float32)
    return (prefix_state + block_state, local_part + carried)

def reference(tokens, w_query, w_key, w_value, w_output):
    results = []
    for batch_row in range(BATCH):
        rows_in = tokens[batch_row]
        queries = jax.nn.silu(jnp.dot(rows_in, w_query, preferred_element_type=jnp.float32)).astype(jnp.bfloat16)
        keys = jax.nn.silu(jnp.dot(rows_in, w_key, preferred_element_type=jnp.float32)).astype(jnp.bfloat16)
        values = jnp.dot(rows_in, w_value, preferred_element_type=jnp.float32).astype(jnp.bfloat16)
        shape_blocks = (LENGTH // TOK_DEV, TOK_DEV, HEADS, HD)
        start_state = jnp.zeros((HEADS, HD, HD), jnp.float32)
        final_state, attended = lax.scan(attend_block, start_state, (queries.reshape(shape_blocks), keys.reshape(shape_blocks), values.reshape(shape_blocks)))
        attended = attended.reshape(LENGTH, HEADS, HD)
        scale = lax.rsqrt(lax.optimization_barrier(jnp.mean(attended * attended, axis=2, keepdims=True)) + 1e-06)
        normed = (attended * scale).reshape(LENGTH, HEADS * HD).astype(jnp.bfloat16)
        results.append(jnp.dot(normed, w_output, preferred_element_type=jnp.float32).astype(jnp.bfloat16))
    return jnp.stack(results, axis=0)
```

```python
import jax
import jax.numpy as jnp
from jax import lax
from jax.sharding import PartitionSpec as P

HD = 128
F32 = jnp.float32
BF16 = jnp.bfloat16


def swap_cores(x):
    return lax.ppermute(x, "wt", [(0, 1), (1, 0)])


def shifted(x, axis, pairs):
    return lax.ppermute(x, axis, pairs)


def prefix_over_seq(state, seq_size):
    nx, ny = 4, 4
    nz = seq_size // (nx * ny)
    i = lax.axis_index("seq")
    x = i % nx
    y = (i // nx) % ny

    def along(value, stride, size, pos):
        sent = value.astype(BF16)
        before = jnp.zeros_like(value)
        total = value
        for d in range(1, size):
            pairs = []
            for j in range(seq_size):
                jp = (j // stride) % size
                pairs.append((j, j + (((jp + d) % size) - jp) * stride))
            got = shifted(sent, "seq", pairs).astype(F32)
            before = before + jnp.where((pos - d) % size < pos, got, 0.0)
            total = total + got
        return before, total

    ex, row_total = along(state, 1, nx, x)
    ey, plane_total = along(row_total, nx, ny, y)
    ez = jnp.zeros_like(state)
    if nz > 1:
        plane = nx * ny
        zpairs = [(j, j + plane) for j in range(seq_size - plane)]
        ez = shifted(plane_total.astype(BF16), "seq", zpairs).astype(F32)
    return ex + ey + ez


def shards(seq_size, tokens, w_query, w_key, w_value, w_output):
    rows_in = tokens.reshape(tokens.shape[1], tokens.shape[2])
    tok_count = rows_in.shape[0]
    half = w_query.shape[0]
    width_local = w_query.shape[1]
    head_count = width_local // HD
    c = lax.axis_index("wt")

    mine_cols = lax.dynamic_slice_in_dim(rows_in, c * half, half, axis=1)
    their_cols = lax.dynamic_slice_in_dim(rows_in, (1 - c) * half, half, axis=1)
    got_cols = swap_cores(their_cols)
    sums = []
    for w in (w_query, w_key, w_value):
        lent = swap_cores(jnp.dot(got_cols, w, preferred_element_type=F32))
        own = jnp.dot(mine_cols, w, preferred_element_type=F32)
        sums.append(own + lent)
    query_sum, key_sum, value_sum = sums

    queries = jax.nn.silu(query_sum).astype(BF16).reshape(tok_count, head_count, HD)
    keys_all = jax.nn.silu(key_sum).astype(BF16).reshape(tok_count, head_count, HD)
    values = value_sum.astype(BF16).reshape(tok_count, head_count, HD)
    local_state = jnp.einsum("thd,the->hde", keys_all, values, preferred_element_type=F32)
    prefix_state = prefix_over_seq(local_state, seq_size)

    scores = jnp.einsum("thd,shd->hts", queries, keys_all, preferred_element_type=F32)
    positions = jnp.arange(tok_count)
    causal = (positions[None, :] <= positions[:, None]).astype(F32)
    scores = (scores * causal[None, :, :]).astype(BF16)
    local_part = jnp.einsum("hts,shd->thd", scores, values, preferred_element_type=F32)
    carried = jnp.einsum(
        "thd,hde->the", queries.astype(F32), prefix_state, precision=lax.Precision.HIGHEST
    )
    attended = local_part + carried
    scale = lax.rsqrt(jnp.mean(attended * attended, axis=2, keepdims=True) + 1e-06)
    normed = (attended * scale).reshape(tok_count, width_local).astype(BF16)

    w_other = swap_cores(w_output)
    y_mine = jnp.dot(normed, w_output, preferred_element_type=F32)
    y_other = jnp.dot(normed, w_other, preferred_element_type=F32)
    quarter = y_mine.shape[1] // 2

    def block(q):
        sub = q % 2
        a = lax.dynamic_slice_in_dim(y_mine, sub * quarter, quarter, axis=1)
        b = lax.dynamic_slice_in_dim(y_other, sub * quarter, quarter, axis=1)
        return jnp.where(q // 2 == c, a, b)

    n = 4
    h = lax.axis_index("head")
    right = jnp.zeros((tok_count, quarter), F32)
    left = jnp.zeros((tok_count, quarter), F32)
    for s in range(1, n):
        qr = jnp.clip(h + n - s, 0, n - 1)
        ql = jnp.clip(h - n + s, 0, n - 1)
        send_r = (block(qr) + right).astype(BF16)
        send_l = (block(ql) + left).astype(BF16)
        rpairs = [(j, j + 1) for j in range(s) if j + 1 < n]
        lpairs = [(j, j - 1) for j in range(n - s, n) if j - 1 >= 0]
        right = lax.ppermute(send_r, "head", rpairs).astype(F32)
        left = lax.ppermute(send_l, "head", lpairs).astype(F32)
    mixed = (block(h) + right + left).astype(BF16)
    return mixed.reshape(1, tok_count, quarter)


def solution(mesh):
    import functools

    placed = (
        P("wt", "seq", None),
        P("wt", "head"),
        P("wt", "head"),
        P("wt", "head"),
        P("head", "wt"),
    )
    return jax.shard_map(
        functools.partial(shards, mesh.shape["seq"]),
        mesh=mesh,
        in_specs=placed,
        out_specs=P("wt", "seq", "head"),
        check_vma=False,
    )
```

```python
import jax
import jax.numpy as jnp
from jax import lax
from jax.sharding import PartitionSpec as P

HD = 128
F32 = jnp.float32
BF16 = jnp.bfloat16


def swap_cores(x):
    return lax.ppermute(x, "wt", [(0, 1), (1, 0)])


def shifted(x, axis, pairs):
    return lax.ppermute(x, axis, pairs)


def prefix_over_seq(state, seq_size):
    nx = 4
    rows = seq_size // nx
    i = lax.axis_index("seq")

    def gather(value, stride, size, pos):
        sent = value.astype(BF16)
        before = jnp.zeros_like(value)
        total = value
        for d in range(1, size):
            pairs = []
            for j in range(seq_size):
                jp = (j // stride) % size
                pairs.append((j, j + (((jp + d) % size) - jp) * stride))
            got = shifted(sent, "seq", pairs).astype(F32)
            before = before + jnp.where((pos - d) % size < pos, got, 0.0)
            total = total + got
        return before, total

    ex, row_total = gather(state, 1, nx, i % nx)
    erow, _ = gather(row_total, nx, rows, i // nx)
    return ex + erow


def shards(seq_size, tokens, w_query, w_key, w_value, w_output):
    rows_in = tokens.reshape(tokens.shape[1], tokens.shape[2])
    tok_count = rows_in.shape[0]
    half = w_query.shape[0]
    width_local = w_query.shape[1]
    head_count = width_local // HD
    c = lax.axis_index("wt")

    mine_cols = lax.dynamic_slice_in_dim(rows_in, c * half, half, axis=1)
    their_cols = lax.dynamic_slice_in_dim(rows_in, (1 - c) * half, half, axis=1)
    got_cols = swap_cores(their_cols)
    sums = []
    for w in (w_query, w_key, w_value):
        lent = swap_cores(jnp.dot(got_cols, w, preferred_element_type=F32))
        own = jnp.dot(mine_cols, w, preferred_element_type=F32)
        sums.append(own + lent)
    query_sum, key_sum, value_sum = sums

    queries = jax.nn.silu(query_sum).astype(BF16).reshape(tok_count, head_count, HD)
    keys_all = jax.nn.silu(key_sum).astype(BF16).reshape(tok_count, head_count, HD)
    values = value_sum.astype(BF16).reshape(tok_count, head_count, HD)
    local_state = jnp.einsum("thd,the->hde", keys_all, values, preferred_element_type=F32)
    prefix_state = prefix_over_seq(local_state, seq_size)

    scores = jnp.einsum("thd,shd->hts", queries, keys_all, preferred_element_type=F32)
    positions = jnp.arange(tok_count)
    causal = (positions[None, :] <= positions[:, None]).astype(F32)
    scores = (scores * causal[None, :, :]).astype(BF16)
    local_part = jnp.einsum("hts,shd->thd", scores, values, preferred_element_type=F32)
    carried = jnp.einsum(
        "thd,hde->the", queries.astype(F32), prefix_state, precision=lax.Precision.HIGHEST
    )
    attended = local_part + carried
    scale = lax.rsqrt(jnp.mean(attended * attended, axis=2, keepdims=True) + 1e-06)
    normed = (attended * scale).reshape(tok_count, width_local).astype(BF16)

    w_other = swap_cores(w_output)
    quarter = w_output.shape[1] // 2
    n = 4
    h = lax.axis_index("head")

    def weight_for(q):
        sub = q % 2
        a = lax.dynamic_slice_in_dim(w_output, sub * quarter, quarter, axis=1)
        b = lax.dynamic_slice_in_dim(w_other, sub * quarter, quarter, axis=1)
        return jnp.where(q // 2 == c, a, b)

    targets = [jnp.clip(h + n - s, 0, n - 1) for s in range(1, n)]
    targets += [jnp.clip(h - n + s, 0, n - 1) for s in range(1, n)]
    targets.append(h)
    picked = lax.optimization_barrier([weight_for(q) for q in targets])
    w_right, w_left, w_own = picked[: n - 1], picked[n - 1 : 2 * n - 2], picked[-1]

    def block(wq):
        return jnp.dot(normed, wq, preferred_element_type=F32)

    right = jnp.zeros((tok_count, quarter), F32)
    left = jnp.zeros((tok_count, quarter), F32)
    for s in range(1, n):
        send_r = (block(w_right[s - 1]) + right).astype(BF16)
        send_l = (block(w_left[s - 1]) + left).astype(BF16)
        rpairs = [(j, j + 1) for j in range(s) if j + 1 < n]
        lpairs = [(j, j - 1) for j in range(n - s, n) if j - 1 >= 0]
        right = lax.ppermute(send_r, "head", rpairs).astype(F32)
        left = lax.ppermute(send_l, "head", lpairs).astype(F32)
    mixed = (block(w_own) + right + left).astype(BF16)
    return mixed.reshape(1, tok_count, quarter)


def solution(mesh):
    import functools

    placed = (
        P("wt", "seq", None),
        P("wt", "head"),
        P("wt", "head"),
        P("wt", "head"),
        P("head", "wt"),
    )
    return jax.shard_map(
        functools.partial(shards, mesh.shape["seq"]),
        mesh=mesh,
        in_specs=placed,
        out_specs=P("wt", "seq", "head"),
        check_vma=False,
    )
```

```python
import jax
import jax.numpy as jnp
from jax import lax
from jax.sharding import PartitionSpec as P

HD = 128
F32 = jnp.float32
BF16 = jnp.bfloat16


def swap_cores(x):
    return lax.ppermute(x, "wt", [(0, 1), (1, 0)])


def shifted(x, axis, pairs):
    return lax.ppermute(x, axis, pairs)


def prefix_over_seq(state, seq_size):
    nx, ny = 4, 4
    nz = seq_size // (nx * ny)
    i = lax.axis_index("seq")
    x = i % nx
    y = (i // nx) % ny

    def along(value, stride, size, pos):
        sent = value.astype(BF16)
        before = jnp.zeros_like(value)
        total = value
        for d in range(1, size):
            pairs = []
            for j in range(seq_size):
                jp = (j // stride) % size
                pairs.append((j, j + (((jp + d) % size) - jp) * stride))
            got = shifted(sent, "seq", pairs).astype(F32)
            before = before + jnp.where((pos - d) % size < pos, got, 0.0)
            total = total + got
        return before, total

    ex, row_total = along(state, 1, nx, x)
    ey, plane_total = along(row_total, nx, ny, y)
    ez = jnp.zeros_like(state)
    if nz > 1:
        plane = nx * ny
        zpairs = [(j, j + plane) for j in range(seq_size - plane)]
        ez = shifted(plane_total.astype(BF16), "seq", zpairs).astype(F32)
    return ex + ey + ez


def shards(seq_size, tokens, w_query, w_key, w_value, w_output):
    rows_in = tokens.reshape(tokens.shape[1], tokens.shape[2])
    tok_count = rows_in.shape[0]
    half = w_query.shape[0]
    width_local = w_query.shape[1]
    head_count = width_local // HD
    c = lax.axis_index("wt")

    mine_cols = lax.dynamic_slice_in_dim(rows_in, c * half, half, axis=1)
    their_cols = lax.dynamic_slice_in_dim(rows_in, (1 - c) * half, half, axis=1)
    got_cols = swap_cores(their_cols)
    sums = []
    for w in (w_query, w_key, w_value):
        lent = swap_cores(jnp.dot(got_cols, w, preferred_element_type=F32))
        own = jnp.dot(mine_cols, w, preferred_element_type=F32)
        sums.append(own + lent)
    query_sum, key_sum, value_sum = sums

    queries = jax.nn.silu(query_sum).astype(BF16).reshape(tok_count, head_count, HD)
    keys_all = jax.nn.silu(key_sum).astype(BF16).reshape(tok_count, head_count, HD)
    values = value_sum.astype(BF16).reshape(tok_count, head_count, HD)
    local_state = jnp.einsum("thd,the->hde", keys_all, values, preferred_element_type=F32)
    prefix_state = prefix_over_seq(local_state, seq_size)

    scores = jnp.einsum("thd,shd->hts", queries, keys_all, preferred_element_type=F32)
    positions = jnp.arange(tok_count)
    causal = (positions[None, :] <= positions[:, None]).astype(F32)
    scores = (scores * causal[None, :, :]).astype(BF16)
    local_part = jnp.einsum("hts,shd->thd", scores, values, preferred_element_type=F32)
    carried = jnp.einsum(
        "thd,hde->the", queries.astype(F32), prefix_state, precision=lax.Precision.HIGHEST
    )
    attended = local_part + carried
    scale = lax.rsqrt(jnp.mean(attended * attended, axis=2, keepdims=True) + 1e-06)
    normed = (attended * scale).reshape(tok_count, width_local).astype(BF16)

    w_other = swap_cores(w_output)
    quarter = w_output.shape[1] // 2
    n = 4
    h = lax.axis_index("head")

    products = jnp.stack(
        [
            jnp.dot(normed, w[:, k * quarter : (k + 1) * quarter], preferred_element_type=F32)
            for w in (w_output, w_other)
            for k in range(2)
        ]
    )

    def block(q):
        k = jnp.where(q // 2 == c, 0, 2) + q % 2
        return lax.dynamic_index_in_dim(products, k, 0, keepdims=False)

    right = jnp.zeros((tok_count, quarter), F32)
    left = jnp.zeros((tok_count, quarter), F32)
    for s in range(1, n):
        qr = jnp.clip(h + n - s, 0, n - 1)
        ql = jnp.clip(h - n + s, 0, n - 1)
        send_r = (block(qr) + right).astype(BF16)
        send_l = (block(ql) + left).astype(BF16)
        rpairs = [(j, j + 1) for j in range(s) if j + 1 < n]
        lpairs = [(j, j - 1) for j in range(n - s, n) if j - 1 >= 0]
        right = lax.ppermute(send_r, "head", rpairs).astype(F32)
        left = lax.ppermute(send_l, "head", lpairs).astype(F32)
    mixed = (block(h) + right + left).astype(BF16)
    return mixed.reshape(1, tok_count, quarter)


def solution(mesh):
    import functools

    placed = (
        P("wt", "seq", None),
        P("wt", "head"),
        P("wt", "head"),
        P("wt", "head"),
        P("head", "wt"),
    )
    return jax.shard_map(
        functools.partial(shards, mesh.shape["seq"]),
        mesh=mesh,
        in_specs=placed,
        out_specs=P("wt", "seq", "head"),
        check_vma=False,
    )
```

```python
import jax
import jax.numpy as jnp
from jax import lax
from jax.sharding import PartitionSpec as P

HD = 128
F32 = jnp.float32
BF16 = jnp.bfloat16


def swap_cores(x):
    return lax.ppermute(x, "wt", [(0, 1), (1, 0)])


def shifted(x, axis, pairs):
    return lax.ppermute(x, axis, pairs)


def prefix_over_seq(state, seq_size):
    nx, ny = 4, 4
    nz = seq_size // (nx * ny)
    i = lax.axis_index("seq")
    x = i % nx
    y = (i // nx) % ny

    def along(value, stride, size, pos):
        sent = value.astype(BF16)
        before = jnp.zeros_like(value)
        total = value
        for d in range(1, size):
            pairs = []
            for j in range(seq_size):
                jp = (j // stride) % size
                pairs.append((j, j + (((jp + d) % size) - jp) * stride))
            got = shifted(sent, "seq", pairs).astype(F32)
            before = before + jnp.where((pos - d) % size < pos, got, 0.0)
            total = total + got
        return before, total

    ex, row_total = along(state, 1, nx, x)
    ey, plane_total = along(row_total, nx, ny, y)
    ez = jnp.zeros_like(state)
    if nz > 1:
        plane = nx * ny
        zpairs = [(j, j + plane) for j in range(seq_size - plane)]
        ez = shifted(plane_total.astype(BF16), "seq", zpairs).astype(F32)
    return ex + ey + ez


def shards(seq_size, tokens, w_query, w_key, w_value, w_output):
    rows_in = tokens.reshape(tokens.shape[1], tokens.shape[2])
    tok_count = rows_in.shape[0]
    half = w_query.shape[0]
    width_local = w_query.shape[1]
    head_count = width_local // HD
    c = lax.axis_index("wt")

    mine_cols = lax.dynamic_slice_in_dim(rows_in, c * half, half, axis=1)
    their_cols = lax.dynamic_slice_in_dim(rows_in, (1 - c) * half, half, axis=1)
    got_cols = swap_cores(their_cols)
    sums = []
    for w in (w_query, w_key, w_value):
        lent = swap_cores(jnp.dot(got_cols, w, preferred_element_type=F32))
        own = jnp.dot(mine_cols, w, preferred_element_type=F32)
        sums.append(own + lent)
    query_sum, key_sum, value_sum = sums

    queries = jax.nn.silu(query_sum).astype(BF16).reshape(tok_count, head_count, HD)
    keys_all = jax.nn.silu(key_sum).astype(BF16).reshape(tok_count, head_count, HD)
    values = value_sum.astype(BF16).reshape(tok_count, head_count, HD)
    local_state = jnp.einsum("thd,the->hde", keys_all, values, preferred_element_type=F32)
    prefix_state = prefix_over_seq(local_state, seq_size)

    scores = jnp.einsum("thd,shd->hts", queries, keys_all, preferred_element_type=F32)
    positions = jnp.arange(tok_count)
    causal = (positions[None, :] <= positions[:, None]).astype(F32)
    scores = (scores * causal[None, :, :]).astype(BF16)
    local_part = jnp.einsum("hts,shd->thd", scores, values, preferred_element_type=F32)
    carried = jnp.einsum(
        "thd,hde->the", queries.astype(F32), prefix_state, precision=lax.Precision.HIGHEST
    )
    attended = local_part + carried
    scale = lax.rsqrt(jnp.mean(attended * attended, axis=2, keepdims=True) + 1e-06)
    normed = (attended * scale).reshape(tok_count, width_local).astype(BF16)

    w_other = swap_cores(w_output)
    quarter = w_output.shape[1] // 2
    n = 4
    h = lax.axis_index("head")

    halves = jnp.stack([w_output, w_other])

    def block(q):
        k = jnp.where(q // 2 == c, 0, 1)
        wq = lax.dynamic_slice(halves, (k, 0, (q % 2) * quarter), (1, halves.shape[1], quarter))[0]
        return jnp.dot(normed, wq, preferred_element_type=F32)

    right = jnp.zeros((tok_count, quarter), F32)
    left = jnp.zeros((tok_count, quarter), F32)
    for s in range(1, n):
        qr = jnp.clip(h + n - s, 0, n - 1)
        ql = jnp.clip(h - n + s, 0, n - 1)
        send_r = (block(qr) + right).astype(BF16)
        send_l = (block(ql) + left).astype(BF16)
        send_r, send_l = lax.optimization_barrier((send_r, send_l))
        rpairs = [(j, j + 1) for j in range(s) if j + 1 < n]
        lpairs = [(j, j - 1) for j in range(n - s, n) if j - 1 >= 0]
        right = lax.ppermute(send_r, "head", rpairs).astype(F32)
        left = lax.ppermute(send_l, "head", lpairs).astype(F32)
    mixed = (block(h) + right + left).astype(BF16)
    return mixed.reshape(1, tok_count, quarter)


def solution(mesh):
    import functools

    placed = (
        P("wt", "seq", None),
        P("wt", "head"),
        P("wt", "head"),
        P("wt", "head"),
        P("head", "wt"),
    )
    return jax.shard_map(
        functools.partial(shards, mesh.shape["seq"]),
        mesh=mesh,
        in_specs=placed,
        out_specs=P("wt", "seq", "head"),
        check_vma=False,
    )
```

```python
import jax
import jax.numpy as jnp
from jax import lax
from jax.sharding import PartitionSpec as P

HD = 128
F32 = jnp.float32
BF16 = jnp.bfloat16


def swap_cores(x):
    return lax.ppermute(x, "wt", [(0, 1), (1, 0)])


def shifted(x, axis, pairs):
    return lax.ppermute(x, axis, pairs)


def prefix_over_seq(state, seq_size):
    nx, ny = 4, 4
    nz = seq_size // (nx * ny)
    i = lax.axis_index("seq")
    x = i % nx
    y = (i // nx) % ny

    def along(value, stride, size, pos):
        sent = value.astype(BF16)
        before = jnp.zeros_like(value)
        total = value
        for d in range(1, size):
            pairs = []
            for j in range(seq_size):
                jp = (j // stride) % size
                pairs.append((j, j + (((jp + d) % size) - jp) * stride))
            got = shifted(sent, "seq", pairs).astype(F32)
            before = before + jnp.where((pos - d) % size < pos, got, 0.0)
            total = total + got
        return before, total

    ex, row_total = along(state, 1, nx, x)
    ey, plane_total = along(row_total, nx, ny, y)
    ez = jnp.zeros_like(state)
    if nz > 1:
        plane = nx * ny
        zpairs = [(j, j + plane) for j in range(seq_size - plane)]
        ez = shifted(plane_total.astype(BF16), "seq", zpairs).astype(F32)
    return ex + ey + ez


def shards(seq_size, tokens, w_query, w_key, w_value, w_output):
    rows_in = tokens.reshape(tokens.shape[1], tokens.shape[2])
    tok_count = rows_in.shape[0]
    half = w_query.shape[0]
    width_local = w_query.shape[1]
    head_count = width_local // HD
    c = lax.axis_index("wt")

    mine_cols = lax.dynamic_slice_in_dim(rows_in, c * half, half, axis=1)
    their_cols = lax.dynamic_slice_in_dim(rows_in, (1 - c) * half, half, axis=1)
    got_cols = swap_cores(their_cols)
    sums = []
    for w in (w_query, w_key, w_value):
        lent = swap_cores(jnp.dot(got_cols, w, preferred_element_type=F32))
        own = jnp.dot(mine_cols, w, preferred_element_type=F32)
        sums.append(own + lent)
    query_sum, key_sum, value_sum = sums

    queries = jax.nn.silu(query_sum).astype(BF16).reshape(tok_count, head_count, HD)
    keys_all = jax.nn.silu(key_sum).astype(BF16).reshape(tok_count, head_count, HD)
    values = value_sum.astype(BF16).reshape(tok_count, head_count, HD)
    local_state = jnp.einsum("thd,the->hde", keys_all, values, preferred_element_type=F32)
    prefix_state = prefix_over_seq(local_state, seq_size)

    scores = jnp.einsum("thd,shd->hts", queries, keys_all, preferred_element_type=F32)
    positions = jnp.arange(tok_count)
    causal = (positions[None, :] <= positions[:, None]).astype(F32)
    scores = (scores * causal[None, :, :]).astype(BF16)
    local_part = jnp.einsum("hts,shd->thd", scores, values, preferred_element_type=F32)
    carried = jnp.einsum(
        "thd,hde->the", queries.astype(F32), prefix_state, precision=lax.Precision.HIGHEST
    )
    attended = local_part + carried
    scale = lax.rsqrt(jnp.mean(attended * attended, axis=2, keepdims=True) + 1e-06)
    normed = (attended * scale).reshape(tok_count, width_local).astype(BF16)

    w_other = swap_cores(w_output)
    quarter = w_output.shape[1] // 2
    n = 4
    h = lax.axis_index("head")

    halves = jnp.stack([w_output, w_other])
    pieces = []
    for o in range(n):
        q = (h + o) % n
        k = jnp.where(q // 2 == c, 0, 1)
        piece = lax.dynamic_slice(halves, (k, 0, (q % 2) * quarter), (1, halves.shape[1], quarter))
        pieces.append(piece[0])
    rotated = jnp.concatenate(pieces, axis=1)
    products = jnp.dot(normed, rotated, preferred_element_type=F32)

    def block(o):
        return products[:, o * quarter : (o + 1) * quarter]

    right = jnp.zeros((tok_count, quarter), F32)
    left = jnp.zeros((tok_count, quarter), F32)
    for s in range(1, n):
        send_r = (block(n - s) + right).astype(BF16)
        send_l = (block(s) + left).astype(BF16)
        send_r, send_l = lax.optimization_barrier((send_r, send_l))
        rpairs = [(j, j + 1) for j in range(s) if j + 1 < n]
        lpairs = [(j, j - 1) for j in range(n - s, n) if j - 1 >= 0]
        right = lax.ppermute(send_r, "head", rpairs).astype(F32)
        left = lax.ppermute(send_l, "head", lpairs).astype(F32)
    mixed = (block(0) + right + left).astype(BF16)
    return mixed.reshape(1, tok_count, quarter)


def solution(mesh):
    import functools

    placed = (
        P("wt", "seq", None),
        P("wt", "head"),
        P("wt", "head"),
        P("wt", "head"),
        P("head", "wt"),
    )
    return jax.shard_map(
        functools.partial(shards, mesh.shape["seq"]),
        mesh=mesh,
        in_specs=placed,
        out_specs=P("wt", "seq", "head"),
        check_vma=False,
    )
```

```python
import jax
import jax.numpy as jnp
from jax import lax
from jax.sharding import PartitionSpec as P

HD = 128
F32 = jnp.float32
BF16 = jnp.bfloat16


def swap_cores(x):
    return lax.ppermute(x, "wt", [(0, 1), (1, 0)])


def shifted(x, axis, pairs):
    return lax.ppermute(x, axis, pairs)


def prefix_over_seq(state, seq_size):
    nx, ny = 4, 4
    nz = seq_size // (nx * ny)
    i = lax.axis_index("seq")
    x = i % nx
    y = (i // nx) % ny

    def along(value, stride, size, pos):
        sent = value.astype(BF16)
        before = jnp.zeros_like(value)
        total = value
        for d in range(1, size):
            pairs = []
            for j in range(seq_size):
                jp = (j // stride) % size
                pairs.append((j, j + (((jp + d) % size) - jp) * stride))
            got = shifted(sent, "seq", pairs).astype(F32)
            before = before + jnp.where((pos - d) % size < pos, got, 0.0)
            total = total + got
        return before, total

    ex, row_total = along(state, 1, nx, x)
    ey, plane_total = along(row_total, nx, ny, y)
    ez = jnp.zeros_like(state)
    if nz > 1:
        plane = nx * ny
        zpairs = [(j, j + plane) for j in range(seq_size - plane)]
        ez = shifted(plane_total.astype(BF16), "seq", zpairs).astype(F32)
    return ex + ey + ez


def shards(seq_size, tokens, w_query, w_key, w_value, w_output):
    rows_in = tokens.reshape(tokens.shape[1], tokens.shape[2])
    tok_count = rows_in.shape[0]
    half = w_query.shape[0]
    width_local = w_query.shape[1]
    head_count = width_local // HD
    c = lax.axis_index("wt")

    mine_cols = lax.dynamic_slice_in_dim(rows_in, c * half, half, axis=1)
    got_cols = lax.dynamic_slice_in_dim(swap_cores(rows_in), c * half, half, axis=1)
    sums = []
    for w in (w_query, w_key, w_value):
        lent = swap_cores(jnp.dot(got_cols, w, preferred_element_type=F32))
        own = jnp.dot(mine_cols, w, preferred_element_type=F32)
        sums.append(own + lent)
    query_sum, key_sum, value_sum = sums

    queries = jax.nn.silu(query_sum).astype(BF16).reshape(tok_count, head_count, HD)
    keys_all = jax.nn.silu(key_sum).astype(BF16).reshape(tok_count, head_count, HD)
    values = value_sum.astype(BF16).reshape(tok_count, head_count, HD)
    local_state = jnp.einsum("thd,the->hde", keys_all, values, preferred_element_type=F32)
    prefix_state = prefix_over_seq(local_state, seq_size)

    scores = jnp.einsum("thd,shd->hts", queries, keys_all, preferred_element_type=F32)
    positions = jnp.arange(tok_count)
    causal = (positions[None, :] <= positions[:, None]).astype(F32)
    scores = (scores * causal[None, :, :]).astype(BF16)
    local_part = jnp.einsum("hts,shd->thd", scores, values, preferred_element_type=F32)
    carried = jnp.einsum(
        "thd,hde->the", queries.astype(F32), prefix_state, precision=lax.Precision.HIGHEST
    )
    attended = local_part + carried
    scale = lax.rsqrt(jnp.mean(attended * attended, axis=2, keepdims=True) + 1e-06)
    normed = (attended * scale).reshape(tok_count, width_local).astype(BF16)

    w_other = swap_cores(w_output)
    quarter = w_output.shape[1] // 2
    n = 4
    h = lax.axis_index("head")

    halves = jnp.stack([w_output, w_other])
    pieces = []
    for o in range(n):
        q = (h + o) % n
        k = jnp.where(q // 2 == c, 0, 1)
        piece = lax.dynamic_slice(halves, (k, 0, (q % 2) * quarter), (1, halves.shape[1], quarter))
        pieces.append(piece[0])
    def block(o):
        return jnp.dot(normed, pieces[o], preferred_element_type=F32)

    right = jnp.zeros((tok_count, quarter), F32)
    left = jnp.zeros((tok_count, quarter), F32)
    for s in range(1, n):
        send_r = (block(n - s) + right).astype(BF16)
        send_l = (block(s) + left).astype(BF16)
        send_r, send_l = lax.optimization_barrier((send_r, send_l))
        rpairs = [(j, j + 1) for j in range(s) if j + 1 < n]
        lpairs = [(j, j - 1) for j in range(n - s, n) if j - 1 >= 0]
        right = lax.ppermute(send_r, "head", rpairs).astype(F32)
        left = lax.ppermute(send_l, "head", lpairs).astype(F32)
    mixed = (block(0) + right + left).astype(BF16)
    return mixed.reshape(1, tok_count, quarter)


def solution(mesh):
    import functools

    placed = (
        P("wt", "seq", None),
        P("wt", "head"),
        P("wt", "head"),
        P("wt", "head"),
        P("head", "wt"),
    )
    return jax.shard_map(
        functools.partial(shards, mesh.shape["seq"]),
        mesh=mesh,
        in_specs=placed,
        out_specs=P("wt", "seq", "head"),
        check_vma=False,
    )
```

```python
import jax
import jax.numpy as jnp
from jax import lax
from jax.sharding import PartitionSpec as P

HD = 128
F32 = jnp.float32
BF16 = jnp.bfloat16


def swap_cores(x):
    return lax.ppermute(x, "wt", [(0, 1), (1, 0)])


def shifted(x, axis, pairs):
    return lax.ppermute(x, axis, pairs)


def prefix_over_seq(state, seq_size):
    nx, ny = 4, 4
    nz = seq_size // (nx * ny)
    i = lax.axis_index("seq")
    x = i % nx
    y = (i // nx) % ny

    def along(value, stride, size, pos):
        sent = value.astype(BF16)
        before = jnp.zeros_like(value)
        total = value
        for d in range(1, size):
            pairs = []
            for j in range(seq_size):
                jp = (j // stride) % size
                pairs.append((j, j + (((jp + d) % size) - jp) * stride))
            got = shifted(sent, "seq", pairs).astype(F32)
            before = before + jnp.where((pos - d) % size < pos, got, 0.0)
            total = total + got
        return before, total

    ex, row_total = along(state, 1, nx, x)
    ey, plane_total = along(row_total, nx, ny, y)
    ez = jnp.zeros_like(state)
    if nz > 1:
        plane = nx * ny
        zpairs = [(j, j + plane) for j in range(seq_size - plane)]
        ez = shifted(plane_total.astype(BF16), "seq", zpairs).astype(F32)
    return ex + ey + ez


def shards(seq_size, tokens, w_query, w_key, w_value, w_output):
    rows_in = tokens.reshape(tokens.shape[1], tokens.shape[2])
    tok_count = rows_in.shape[0]
    half = w_query.shape[0]
    width_local = w_query.shape[1]
    head_count = width_local // HD
    c = lax.axis_index("wt")

    mine_cols = lax.dynamic_slice_in_dim(rows_in, c * half, half, axis=1)
    their_cols = lax.dynamic_slice_in_dim(rows_in, (1 - c) * half, half, axis=1)
    got_cols = swap_cores(their_cols)
    sums = []
    for w in (w_query, w_key, w_value):
        lent = swap_cores(jnp.dot(got_cols, w, preferred_element_type=F32))
        own = jnp.dot(mine_cols, w, preferred_element_type=F32)
        sums.append(own + lent)
    query_sum, key_sum, value_sum = sums

    queries = jax.nn.silu(query_sum).astype(BF16).reshape(tok_count, head_count, HD)
    keys_all = jax.nn.silu(key_sum).astype(BF16).reshape(tok_count, head_count, HD)
    values = value_sum.astype(BF16).reshape(tok_count, head_count, HD)
    local_state = jnp.einsum("thd,the->hde", keys_all, values, preferred_element_type=F32)
    prefix_state = prefix_over_seq(local_state, seq_size)

    scores = jnp.einsum("thd,shd->hts", queries, keys_all, preferred_element_type=F32)
    positions = jnp.arange(tok_count)
    causal = (positions[None, :] <= positions[:, None]).astype(F32)
    scores = (scores * causal[None, :, :]).astype(BF16)
    local_part = jnp.einsum("hts,shd->thd", scores, values, preferred_element_type=F32)
    carried = jnp.einsum(
        "thd,hde->the", queries.astype(F32), prefix_state.astype(BF16).astype(F32), preferred_element_type=F32
    )
    attended = local_part + carried
    scale = lax.rsqrt(jnp.mean(attended * attended, axis=2, keepdims=True) + 1e-06)
    normed = (attended * scale).reshape(tok_count, width_local).astype(BF16)

    w_other = swap_cores(w_output)
    quarter = w_output.shape[1] // 2
    n = 4
    h = lax.axis_index("head")

    halves = jnp.stack([w_output, w_other])
    pieces = []
    for o in range(n):
        q = (h + o) % n
        k = jnp.where(q // 2 == c, 0, 1)
        piece = lax.dynamic_slice(halves, (k, 0, (q % 2) * quarter), (1, halves.shape[1], quarter))
        pieces.append(piece[0])
    rotated = jnp.concatenate(pieces, axis=1)
    products = jnp.dot(normed, rotated, preferred_element_type=F32)

    def block(o):
        return products[:, o * quarter : (o + 1) * quarter]

    right = jnp.zeros((tok_count, quarter), F32)
    left = jnp.zeros((tok_count, quarter), F32)
    for s in range(1, n):
        send_r = (block(n - s) + right).astype(BF16)
        send_l = (block(s) + left).astype(BF16)
        send_r, send_l = lax.optimization_barrier((send_r, send_l))
        rpairs = [(j, j + 1) for j in range(s) if j + 1 < n]
        lpairs = [(j, j - 1) for j in range(n - s, n) if j - 1 >= 0]
        right = lax.ppermute(send_r, "head", rpairs).astype(F32)
        left = lax.ppermute(send_l, "head", lpairs).astype(F32)
    mixed = (block(0) + right + left).astype(BF16)
    return mixed.reshape(1, tok_count, quarter)


def solution(mesh):
    import functools

    placed = (
        P("wt", "seq", None),
        P("wt", "head"),
        P("wt", "head"),
        P("wt", "head"),
        P("head", "wt"),
    )
    return jax.shard_map(
        functools.partial(shards, mesh.shape["seq"]),
        mesh=mesh,
        in_specs=placed,
        out_specs=P("wt", "seq", "head"),
        check_vma=False,
    )
```

```python
import jax
import jax.numpy as jnp
from jax import lax
from jax.sharding import PartitionSpec as P

HD = 128
F32 = jnp.float32
BF16 = jnp.bfloat16


def swap_cores(x):
    return lax.ppermute(x, "wt", [(0, 1), (1, 0)])


def shifted(x, axis, pairs):
    return lax.ppermute(x, axis, pairs)


def prefix_over_seq(state, seq_size):
    nx, ny = 4, 4
    nz = seq_size // (nx * ny)
    i = lax.axis_index("seq")
    x = i % nx
    y = (i // nx) % ny

    def along(value, stride, size, pos):
        sent = value.astype(BF16)
        before = jnp.zeros_like(value)
        total = value
        for d in range(1, size):
            pairs = []
            for j in range(seq_size):
                jp = (j // stride) % size
                pairs.append((j, j + (((jp + d) % size) - jp) * stride))
            got = shifted(sent, "seq", pairs).astype(F32)
            before = before + jnp.where((pos - d) % size < pos, got, 0.0)
            total = total + got
        return before, total

    ex, row_total = along(state, 1, nx, x)
    ey, plane_total = along(row_total, nx, ny, y)
    ez = jnp.zeros_like(state)
    if nz > 1:
        plane = nx * ny
        zpairs = [(j, j + plane) for j in range(seq_size - plane)]
        ez = shifted(plane_total.astype(BF16), "seq", zpairs).astype(F32)
    return ex + ey + ez


def shards(seq_size, tokens, w_query, w_key, w_value, w_output):
    rows_in = tokens.reshape(tokens.shape[1], tokens.shape[2])
    tok_count = rows_in.shape[0]
    half = w_query.shape[0]
    width_local = w_query.shape[1]
    head_count = width_local // HD
    c = lax.axis_index("wt")

    mine_cols = lax.dynamic_slice_in_dim(rows_in, c * half, half, axis=1)
    got_cols = lax.dynamic_slice_in_dim(swap_cores(rows_in), c * half, half, axis=1)
    sums = []
    for w in (w_query, w_key, w_value):
        lent = swap_cores(jnp.dot(got_cols, w, preferred_element_type=F32))
        own = jnp.dot(mine_cols, w, preferred_element_type=F32)
        sums.append(own + lent)
    query_sum, key_sum, value_sum = sums

    queries = jax.nn.silu(query_sum).astype(BF16).reshape(tok_count, head_count, HD)
    keys_all = jax.nn.silu(key_sum).astype(BF16).reshape(tok_count, head_count, HD)
    values = value_sum.astype(BF16).reshape(tok_count, head_count, HD)
    local_state = jnp.einsum("thd,the->hde", keys_all, values, preferred_element_type=F32)
    prefix_state = prefix_over_seq(local_state, seq_size)

    scores = jnp.einsum("thd,shd->hts", queries, keys_all, preferred_element_type=F32)
    positions = jnp.arange(tok_count)
    causal = (positions[None, :] <= positions[:, None]).astype(F32)
    scores = (scores * causal[None, :, :]).astype(BF16)
    local_part = jnp.einsum("hts,shd->thd", scores, values, preferred_element_type=F32)
    carried = jnp.einsum(
        "thd,hde->the", queries.astype(F32), prefix_state.astype(BF16).astype(F32), preferred_element_type=F32
    )
    attended = local_part + carried
    scale = lax.rsqrt(jnp.mean(attended * attended, axis=2, keepdims=True) + 1e-06)
    normed = (attended * scale).reshape(tok_count, width_local).astype(BF16)

    w_other = swap_cores(w_output)
    quarter = w_output.shape[1] // 2
    n = 4
    h = lax.axis_index("head")

    halves = jnp.stack([w_output, w_other])
    pieces = []
    for o in range(n):
        q = (h + o) % n
        k = jnp.where(q // 2 == c, 0, 1)
        piece = lax.dynamic_slice(halves, (k, 0, (q % 2) * quarter), (1, halves.shape[1], quarter))
        pieces.append(piece[0])
    rotated = jnp.concatenate(pieces, axis=1)
    products = jnp.dot(normed, rotated, preferred_element_type=F32)

    def block(o):
        return products[:, o * quarter : (o + 1) * quarter]

    right = jnp.zeros((tok_count, quarter), F32)
    left = jnp.zeros((tok_count, quarter), F32)
    for s in range(1, n):
        send_r = (block(n - s) + right).astype(BF16)
        send_l = (block(s) + left).astype(BF16)
        send_r, send_l = lax.optimization_barrier((send_r, send_l))
        rpairs = [(j, j + 1) for j in range(s) if j + 1 < n]
        lpairs = [(j, j - 1) for j in range(n - s, n) if j - 1 >= 0]
        right = lax.ppermute(send_r, "head", rpairs).astype(F32)
        left = lax.ppermute(send_l, "head", lpairs).astype(F32)
    mixed = (block(0) + right + left).astype(BF16)
    return mixed.reshape(1, tok_count, quarter)


def solution(mesh):
    import functools

    placed = (
        P("wt", "seq", None),
        P("wt", "head"),
        P("wt", "head"),
        P("wt", "head"),
        P("head", "wt"),
    )
    return jax.shard_map(
        functools.partial(shards, mesh.shape["seq"]),
        mesh=mesh,
        in_specs=placed,
        out_specs=P("wt", "seq", "head"),
        check_vma=False,
    )
```

```python
import jax
import jax.numpy as jnp
from jax import lax
from jax.sharding import PartitionSpec as P

HD = 128
F32 = jnp.float32
BF16 = jnp.bfloat16


def swap_cores(x):
    return lax.ppermute(x, "wt", [(0, 1), (1, 0)])


def shifted(x, axis, pairs):
    return lax.ppermute(x, axis, pairs)


def prefix_over_seq(state, seq_size):
    nx, ny = 4, 4
    nz = seq_size // (nx * ny)
    i = lax.axis_index("seq")
    x = i % nx
    y = (i // nx) % ny

    def along(value, stride, size, pos):
        sent = value.astype(BF16)
        before = jnp.zeros_like(value)
        total = value
        for d in range(1, size):
            pairs = []
            for j in range(seq_size):
                jp = (j // stride) % size
                pairs.append((j, j + (((jp + d) % size) - jp) * stride))
            got = shifted(sent, "seq", pairs).astype(F32)
            before = before + jnp.where((pos - d) % size < pos, got, 0.0)
            total = total + got
        return before, total

    ex, row_total = along(state, 1, nx, x)
    ey, plane_total = along(row_total, nx, ny, y)
    ez = jnp.zeros_like(state)
    if nz > 1:
        plane = nx * ny
        zpairs = [(j, j + plane) for j in range(seq_size - plane)]
        ez = shifted(plane_total.astype(BF16), "seq", zpairs).astype(F32)
    return ex + ey + ez


def shards(seq_size, tokens, w_query, w_key, w_value, w_output):
    rows_in = tokens.reshape(tokens.shape[1], tokens.shape[2])
    tok_count = rows_in.shape[0]
    half = w_query.shape[0]
    width_local = w_query.shape[1]
    head_count = width_local // HD
    c = lax.axis_index("wt")

    both_rows = jnp.concatenate([rows_in, swap_cores(rows_in)], axis=0)
    both_cols = lax.dynamic_slice_in_dim(both_rows, c * half, half, axis=1)
    sums = []
    for w in (w_key, w_value, w_query):
        part = jnp.dot(both_cols, w, preferred_element_type=F32)
        sums.append(part[:tok_count] + swap_cores(part[tok_count:]))
    key_sum, value_sum, query_sum = sums

    queries = jax.nn.silu(query_sum).astype(BF16).reshape(tok_count, head_count, HD)
    keys_all = jax.nn.silu(key_sum).astype(BF16).reshape(tok_count, head_count, HD)
    values = value_sum.astype(BF16).reshape(tok_count, head_count, HD)
    local_state = jnp.einsum("thd,the->hde", keys_all, values, preferred_element_type=F32)
    prefix_state = prefix_over_seq(local_state, seq_size)

    scores = jnp.einsum("thd,shd->hts", queries, keys_all, preferred_element_type=F32)
    positions = jnp.arange(tok_count)
    causal = (positions[None, :] <= positions[:, None]).astype(F32)
    scores = (scores * causal[None, :, :]).astype(BF16)
    local_part = jnp.einsum("hts,shd->thd", scores, values, preferred_element_type=F32)
    carried = jnp.einsum(
        "thd,hde->the", queries.astype(F32), prefix_state.astype(BF16).astype(F32), preferred_element_type=F32
    )
    attended = local_part + carried
    scale = lax.rsqrt(jnp.mean(attended * attended, axis=2, keepdims=True) + 1e-06)
    normed = (attended * scale).reshape(tok_count, width_local).astype(BF16)

    w_other = swap_cores(w_output)
    quarter = w_output.shape[1] // 2
    n = 4
    h = lax.axis_index("head")

    halves = jnp.stack([w_output, w_other])
    pieces = []
    for o in range(n):
        q = (h + o) % n
        k = jnp.where(q // 2 == c, 0, 1)
        piece = lax.dynamic_slice(halves, (k, 0, (q % 2) * quarter), (1, halves.shape[1], quarter))
        pieces.append(piece[0])
    rotated = jnp.concatenate(pieces, axis=1)
    products = jnp.dot(normed, rotated, preferred_element_type=F32)

    def block(o):
        return products[:, o * quarter : (o + 1) * quarter]

    right = jnp.zeros((tok_count, quarter), F32)
    left = jnp.zeros((tok_count, quarter), F32)
    for s in range(1, n):
        send_r = (block(n - s) + right).astype(BF16)
        send_l = (block(s) + left).astype(BF16)
        send_r, send_l = lax.optimization_barrier((send_r, send_l))
        rpairs = [(j, j + 1) for j in range(s) if j + 1 < n]
        lpairs = [(j, j - 1) for j in range(n - s, n) if j - 1 >= 0]
        right = lax.ppermute(send_r, "head", rpairs).astype(F32)
        left = lax.ppermute(send_l, "head", lpairs).astype(F32)
    mixed = (block(0) + right + left).astype(BF16)
    return mixed.reshape(1, tok_count, quarter)


def solution(mesh):
    import functools

    placed = (
        P("wt", "seq", None),
        P("wt", "head"),
        P("wt", "head"),
        P("wt", "head"),
        P("head", "wt"),
    )
    return jax.shard_map(
        functools.partial(shards, mesh.shape["seq"]),
        mesh=mesh,
        in_specs=placed,
        out_specs=P("wt", "seq", "head"),
        check_vma=False,
    )
```

```python
import jax
import jax.numpy as jnp
from jax import lax
from jax.sharding import PartitionSpec as P

HD = 128
F32 = jnp.float32
BF16 = jnp.bfloat16


def swap_cores(x):
    return lax.ppermute(x, "wt", [(0, 1), (1, 0)])


def shifted(x, axis, pairs):
    return lax.ppermute(x, axis, pairs)


def prefix_over_seq(state, seq_size):
    nx, ny = 4, 4
    nz = seq_size // (nx * ny)
    i = lax.axis_index("seq")
    x = i % nx
    y = (i // nx) % ny

    def along(value, stride, size, pos):
        sent = value.astype(BF16)
        before = jnp.zeros_like(value)
        total = value
        for d in range(1, size):
            pairs = []
            for j in range(seq_size):
                jp = (j // stride) % size
                pairs.append((j, j + (((jp + d) % size) - jp) * stride))
            got = shifted(sent, "seq", pairs).astype(F32)
            before = before + jnp.where((pos - d) % size < pos, got, 0.0)
            total = total + got
        return before, total

    ex, row_total = along(state, 1, nx, x)
    ey, plane_total = along(row_total, nx, ny, y)
    ez = jnp.zeros_like(state)
    if nz > 1:
        plane = nx * ny
        zpairs = [(j, j + plane) for j in range(seq_size - plane)]
        ez = shifted(plane_total.astype(BF16), "seq", zpairs).astype(F32)
    return ex + ey + ez


def shards(seq_size, tokens, w_query, w_key, w_value, w_output):
    rows_in = tokens.reshape(tokens.shape[1], tokens.shape[2])
    tok_count = rows_in.shape[0]
    half = w_query.shape[0]
    width_local = w_query.shape[1]
    head_count = width_local // HD
    c = lax.axis_index("wt")

    mine_cols = lax.dynamic_slice_in_dim(rows_in, c * half, half, axis=1)
    got_cols = lax.dynamic_slice_in_dim(swap_cores(rows_in), c * half, half, axis=1)
    sums = []
    for w in (w_query, w_key, w_value):
        lent = swap_cores(jnp.dot(got_cols, w, preferred_element_type=F32))
        own = jnp.dot(mine_cols, w, preferred_element_type=F32)
        sums.append(own + lent)
    query_sum, key_sum, value_sum = sums

    queries = jax.nn.silu(query_sum).astype(BF16).reshape(tok_count, head_count, HD)
    keys_all = jax.nn.silu(key_sum).astype(BF16).reshape(tok_count, head_count, HD)
    values = value_sum.astype(BF16).reshape(tok_count, head_count, HD)
    local_state = jnp.einsum("thd,the->hde", keys_all, values, preferred_element_type=F32)
    prefix_state = prefix_over_seq(local_state, seq_size)

    scores = jnp.einsum("thd,shd->hts", queries, keys_all, preferred_element_type=F32)
    positions = jnp.arange(tok_count)
    causal = (positions[None, :] <= positions[:, None]).astype(F32)
    scores = (scores * causal[None, :, :]).astype(BF16)
    local_part = jnp.einsum("hts,shd->thd", scores, values, preferred_element_type=F32)
    carried = jnp.einsum(
        "thd,hde->the", queries.astype(F32), prefix_state.astype(BF16).astype(F32), preferred_element_type=F32
    )
    attended = local_part + carried
    scale = lax.rsqrt(jnp.mean(attended * attended, axis=2, keepdims=True) + 1e-06)
    normed = (attended * scale).reshape(tok_count, width_local).astype(BF16)

    w_other = swap_cores(w_output)
    quarter = w_output.shape[1] // 2
    n = 4
    h = lax.axis_index("head")

    halves = jnp.stack([w_output, w_other])
    pieces = []
    for o in range(n):
        q = (h + o) % n
        k = jnp.where(q // 2 == c, 0, 1)
        piece = lax.dynamic_slice(halves, (k, 0, (q % 2) * quarter), (1, halves.shape[1], quarter))
        pieces.append(piece[0])
    rotated = jnp.concatenate(pieces, axis=1)
    products = jnp.dot(normed, rotated, preferred_element_type=F32)

    def block(o):
        return products[:, o * quarter : (o + 1) * quarter]

    part = quarter // 2
    outs = []
    rights = [jnp.zeros((tok_count, part), F32) for _ in range(2)]
    lefts = [jnp.zeros((tok_count, part), F32) for _ in range(2)]

    def piece(o, g):
        return products[:, o * quarter + g * part : o * quarter + (g + 1) * part]

    for s in range(1, n):
        rpairs = [(j, j + 1) for j in range(s) if j + 1 < n]
        lpairs = [(j, j - 1) for j in range(n - s, n) if j - 1 >= 0]
        for g in range(2):
            send_r = (piece(n - s, g) + rights[g]).astype(BF16)
            send_l = (piece(s, g) + lefts[g]).astype(BF16)
            send_r, send_l = lax.optimization_barrier((send_r, send_l))
            rights[g] = lax.ppermute(send_r, "head", rpairs).astype(F32)
            lefts[g] = lax.ppermute(send_l, "head", lpairs).astype(F32)
    for g in range(2):
        outs.append(piece(0, g) + rights[g] + lefts[g])
    mixed = jnp.concatenate(outs, axis=1).astype(BF16)
    return mixed.reshape(1, tok_count, quarter)


def solution(mesh):
    import functools

    placed = (
        P("wt", "seq", None),
        P("wt", "head"),
        P("wt", "head"),
        P("wt", "head"),
        P("head", "wt"),
    )
    return jax.shard_map(
        functools.partial(shards, mesh.shape["seq"]),
        mesh=mesh,
        in_specs=placed,
        out_specs=P("wt", "seq", "head"),
        check_vma=False,
    )
```

```python
import jax
import jax.numpy as jnp
from jax import lax
from jax.sharding import PartitionSpec as P

HD = 128
F32 = jnp.float32
BF16 = jnp.bfloat16


def swap_cores(x):
    return lax.ppermute(x, "wt", [(0, 1), (1, 0)])


def shifted(x, axis, pairs):
    return lax.ppermute(x, axis, pairs)


def prefix_over_seq(state):
    def along(value, axis):
        size = lax.psum(1, axis)
        pos = lax.axis_index(axis)
        sent = jnp.broadcast_to(value.astype(BF16)[None], (size,) + value.shape)
        got = lax.all_to_all(sent, axis, 0, 0).astype(F32)
        order = lax.broadcasted_iota(jnp.int32, (size,) + (1,) * value.ndim, 0)
        before = jnp.sum(jnp.where(order < pos, got, 0.0), axis=0)
        total = jnp.sum(got, axis=0)
        return before, total

    ex, row_total = along(state, "x")
    ey, plane_total = along(row_total, "y")
    nz = lax.psum(1, "zh")
    ez = lax.ppermute(plane_total.astype(BF16), "zh", [(j, j + 1) for j in range(nz - 1)]).astype(F32)
    return ex + ey + ez


def shards(tokens, w_query, w_key, w_value, w_output):
    rows_in = tokens.reshape(tokens.shape[1], tokens.shape[2])
    tok_count = rows_in.shape[0]
    half = w_query.shape[0]
    width_local = w_query.shape[1]
    head_count = width_local // HD
    c = lax.axis_index("wt")

    mine_cols = lax.dynamic_slice_in_dim(rows_in, c * half, half, axis=1)
    got_cols = lax.dynamic_slice_in_dim(swap_cores(rows_in), c * half, half, axis=1)
    sums = []
    for w in (w_query, w_key, w_value):
        lent = swap_cores(jnp.dot(got_cols, w, preferred_element_type=F32))
        own = jnp.dot(mine_cols, w, preferred_element_type=F32)
        sums.append(own + lent)
    query_sum, key_sum, value_sum = sums

    queries = jax.nn.silu(query_sum).astype(BF16).reshape(tok_count, head_count, HD)
    keys_all = jax.nn.silu(key_sum).astype(BF16).reshape(tok_count, head_count, HD)
    values = value_sum.astype(BF16).reshape(tok_count, head_count, HD)
    local_state = jnp.einsum("thd,the->hde", keys_all, values, preferred_element_type=F32)
    prefix_state = prefix_over_seq(local_state)

    scores = jnp.einsum("thd,shd->hts", queries, keys_all, preferred_element_type=F32)
    positions = jnp.arange(tok_count)
    causal = (positions[None, :] <= positions[:, None]).astype(F32)
    scores = (scores * causal[None, :, :]).astype(BF16)
    local_part = jnp.einsum("hts,shd->thd", scores, values, preferred_element_type=F32)
    carried = jnp.einsum(
        "thd,hde->the", queries.astype(F32), prefix_state.astype(BF16).astype(F32), preferred_element_type=F32
    )
    attended = local_part + carried
    scale = lax.rsqrt(jnp.mean(attended * attended, axis=2, keepdims=True) + 1e-06)
    normed = (attended * scale).reshape(tok_count, width_local).astype(BF16)

    w_other = swap_cores(w_output)
    quarter = w_output.shape[1] // 2
    n = 4
    h = lax.axis_index("head")

    halves = jnp.stack([w_output, w_other])
    pieces = []
    for o in range(n):
        q = (h + o) % n
        k = jnp.where(q // 2 == c, 0, 1)
        piece = lax.dynamic_slice(halves, (k, 0, (q % 2) * quarter), (1, halves.shape[1], quarter))
        pieces.append(piece[0])
    rotated = jnp.concatenate(pieces, axis=1)
    products = jnp.dot(normed, rotated, preferred_element_type=F32)

    def block(o):
        return products[:, o * quarter : (o + 1) * quarter]

    right = jnp.zeros((tok_count, quarter), F32)
    left = jnp.zeros((tok_count, quarter), F32)
    for s in range(1, n):
        send_r = (block(n - s) + right).astype(BF16)
        send_l = (block(s) + left).astype(BF16)
        send_r, send_l = lax.optimization_barrier((send_r, send_l))
        rpairs = [(j, j + 1) for j in range(s) if j + 1 < n]
        lpairs = [(j, j - 1) for j in range(n - s, n) if j - 1 >= 0]
        right = lax.ppermute(send_r, "head", rpairs).astype(F32)
        left = lax.ppermute(send_l, "head", lpairs).astype(F32)
    mixed = (block(0) + right + left).astype(BF16)
    return mixed.reshape(1, tok_count, quarter)


def solution(mesh):
    from jax.sharding import Mesh

    seq_size = mesh.shape["seq"]
    nz = seq_size // 16
    split = Mesh(
        mesh.devices.reshape(nz, 4, 4, mesh.shape["wt"], mesh.shape["head"]),
        ("zh", "y", "x", "wt", "head"),
    )
    seq = ("zh", "y", "x")
    placed = (
        P("wt", seq, None),
        P("wt", "head"),
        P("wt", "head"),
        P("wt", "head"),
        P("head", "wt"),
    )
    return jax.shard_map(
        shards,
        mesh=split,
        in_specs=placed,
        out_specs=P("wt", seq, "head"),
        check_vma=False,
    )
```

```python
import jax
import jax.numpy as jnp
from jax import lax
from jax.sharding import PartitionSpec as P

HD = 128
F32 = jnp.float32
BF16 = jnp.bfloat16


def swap_cores(x):
    return lax.ppermute(x, "wt", [(0, 1), (1, 0)])


def shifted(x, axis, pairs):
    return lax.ppermute(x, axis, pairs)


def prefix_over_seq(state, seq_size):
    nx, ny = 4, 4
    nz = seq_size // (nx * ny)
    i = lax.axis_index("seq")
    x = i % nx
    y = (i // nx) % ny

    def along(value, stride, size, pos):
        sent = value.astype(BF16)
        before = jnp.zeros_like(value)
        total = value
        for d in range(1, size):
            pairs = []
            for j in range(seq_size):
                jp = (j // stride) % size
                pairs.append((j, j + (((jp + d) % size) - jp) * stride))
            got = shifted(sent, "seq", pairs).astype(F32)
            before = before + jnp.where((pos - d) % size < pos, got, 0.0)
            total = total + got
        return before, total

    ex, row_total = along(state, 1, nx, x)
    ey, plane_total = along(row_total, nx, ny, y)
    ez = jnp.zeros_like(state)
    if nz > 1:
        plane = nx * ny
        zpairs = [(j, j + plane) for j in range(seq_size - plane)]
        ez = shifted(plane_total.astype(BF16), "seq", zpairs).astype(F32)
    return ex + ey + ez


def shards(seq_size, tokens, w_query, w_key, w_value, w_output):
    rows_in = tokens.reshape(tokens.shape[1], tokens.shape[2])
    tok_count = rows_in.shape[0]
    half = w_query.shape[0]
    width_local = w_query.shape[1]
    head_count = width_local // HD
    c = lax.axis_index("wt")

    mine_cols = lax.dynamic_slice_in_dim(rows_in, c * half, half, axis=1)
    got_cols = lax.dynamic_slice_in_dim(swap_cores(rows_in), c * half, half, axis=1)
    sums = []
    for w in (w_query, w_key, w_value):
        lent = swap_cores(jnp.dot(got_cols, w, preferred_element_type=F32))
        own = jnp.dot(mine_cols, w, preferred_element_type=F32)
        sums.append(own + lent)
    query_sum, key_sum, value_sum = sums

    queries = jax.nn.silu(query_sum).astype(BF16).reshape(tok_count, head_count, HD)
    keys_all = jax.nn.silu(key_sum).astype(BF16).reshape(tok_count, head_count, HD)
    values = value_sum.astype(BF16).reshape(tok_count, head_count, HD)
    local_state = jnp.einsum("thd,the->hde", keys_all, values, preferred_element_type=F32)
    prefix_state = prefix_over_seq(local_state, seq_size)

    scores = jnp.einsum("thd,shd->hts", queries, keys_all, preferred_element_type=F32)
    positions = jnp.arange(tok_count)
    causal = (positions[None, :] <= positions[:, None]).astype(F32)
    scores = (scores * causal[None, :, :]).astype(BF16)
    local_part = jnp.einsum("hts,shd->thd", scores, values, preferred_element_type=F32)
    carried = jnp.einsum(
        "thd,hde->the", queries.astype(F32), prefix_state.astype(BF16).astype(F32), preferred_element_type=F32
    )
    attended = local_part + carried
    scale = lax.rsqrt(jnp.mean(attended * attended, axis=2, keepdims=True) + 1e-06)
    normed = (attended * scale).reshape(tok_count, width_local).astype(BF16)

    w_other = swap_cores(w_output)
    quarter = w_output.shape[1] // 2
    n = 4
    h = lax.axis_index("head")

    halves = jnp.stack([w_output, w_other])
    pieces = []
    for o in range(n):
        q = (h + o) % n
        k = jnp.where(q // 2 == c, 0, 1)
        piece = lax.dynamic_slice(halves, (k, 0, (q % 2) * quarter), (1, halves.shape[1], quarter))
        pieces.append(piece[0])
    early = jnp.dot(normed, jnp.concatenate([pieces[3], pieces[1]], axis=1), preferred_element_type=F32)
    late = jnp.dot(normed, jnp.concatenate([pieces[2], pieces[0]], axis=1), preferred_element_type=F32)
    where_is = {3: (early, 0), 1: (early, 1), 2: (late, 0), 0: (late, 1)}

    def block(o):
        held, k = where_is[o]
        return held[:, k * quarter : (k + 1) * quarter]

    right = jnp.zeros((tok_count, quarter), F32)
    left = jnp.zeros((tok_count, quarter), F32)
    for s in range(1, n):
        send_r = (block(n - s) + right).astype(BF16)
        send_l = (block(s) + left).astype(BF16)
        send_r, send_l = lax.optimization_barrier((send_r, send_l))
        rpairs = [(j, j + 1) for j in range(s) if j + 1 < n]
        lpairs = [(j, j - 1) for j in range(n - s, n) if j - 1 >= 0]
        right = lax.ppermute(send_r, "head", rpairs).astype(F32)
        left = lax.ppermute(send_l, "head", lpairs).astype(F32)
    mixed = (block(0) + right + left).astype(BF16)
    return mixed.reshape(1, tok_count, quarter)


def solution(mesh):
    import functools

    placed = (
        P("wt", "seq", None),
        P("wt", "head"),
        P("wt", "head"),
        P("wt", "head"),
        P("head", "wt"),
    )
    return jax.shard_map(
        functools.partial(shards, mesh.shape["seq"]),
        mesh=mesh,
        in_specs=placed,
        out_specs=P("wt", "seq", "head"),
        check_vma=False,
    )
```

```python
import jax
import jax.numpy as jnp
from jax import lax
from jax.sharding import PartitionSpec as P

HD = 128
F32 = jnp.float32
BF16 = jnp.bfloat16


def swap_cores(x):
    return lax.ppermute(x, "wt", [(0, 1), (1, 0)])


def shifted(x, axis, pairs):
    return lax.ppermute(x, axis, pairs)


def prefix_over_seq(state, seq_size):
    nx, ny = 4, 4
    nz = seq_size // (nx * ny)
    i = lax.axis_index("seq")
    x = i % nx
    y = (i // nx) % ny

    def along(value, stride, size, pos):
        sent = value.astype(BF16)
        before = jnp.zeros_like(value)
        total = value
        for d in range(1, size):
            pairs = []
            for j in range(seq_size):
                jp = (j // stride) % size
                pairs.append((j, j + (((jp + d) % size) - jp) * stride))
            got = shifted(sent, "seq", pairs).astype(F32)
            before = before + jnp.where((pos - d) % size < pos, got, 0.0)
            total = total + got
        return before, total

    ex, row_total = along(state, 1, nx, x)
    ey, plane_total = along(row_total, nx, ny, y)
    ez = jnp.zeros_like(state)
    if nz > 1:
        plane = nx * ny
        zpairs = [(j, j + plane) for j in range(seq_size - plane)]
        ez = shifted(plane_total.astype(BF16), "seq", zpairs).astype(F32)
    return ex + ey + ez


def shards(seq_size, tokens, w_query, w_key, w_value, w_output):
    rows_in = tokens.reshape(tokens.shape[1], tokens.shape[2])
    tok_count = rows_in.shape[0]
    half = w_query.shape[0]
    width_local = w_query.shape[1]
    head_count = width_local // HD
    c = lax.axis_index("wt")

    mine_cols = lax.dynamic_slice_in_dim(rows_in, c * half, half, axis=1)
    got_cols = lax.dynamic_slice_in_dim(swap_cores(rows_in), c * half, half, axis=1)
    kv_lent = swap_cores(
        jnp.concatenate([jnp.dot(got_cols, w, preferred_element_type=F32) for w in (w_key, w_value)], axis=1)
    )
    key_sum = jnp.dot(mine_cols, w_key, preferred_element_type=F32) + kv_lent[:, :width_local]
    value_sum = jnp.dot(mine_cols, w_value, preferred_element_type=F32) + kv_lent[:, width_local:]
    query_sum = jnp.dot(mine_cols, w_query, preferred_element_type=F32) + swap_cores(
        jnp.dot(got_cols, w_query, preferred_element_type=F32)
    )

    queries = jax.nn.silu(query_sum).astype(BF16).reshape(tok_count, head_count, HD)
    keys_all = jax.nn.silu(key_sum).astype(BF16).reshape(tok_count, head_count, HD)
    values = value_sum.astype(BF16).reshape(tok_count, head_count, HD)
    local_state = jnp.einsum("thd,the->hde", keys_all, values, preferred_element_type=F32)
    prefix_state = prefix_over_seq(local_state, seq_size)

    scores = jnp.einsum("thd,shd->hts", queries, keys_all, preferred_element_type=F32)
    positions = jnp.arange(tok_count)
    causal = (positions[None, :] <= positions[:, None]).astype(F32)
    scores = (scores * causal[None, :, :]).astype(BF16)
    local_part = jnp.einsum("hts,shd->thd", scores, values, preferred_element_type=F32)
    carried = jnp.einsum(
        "thd,hde->the", queries.astype(F32), prefix_state.astype(BF16).astype(F32), preferred_element_type=F32
    )
    attended = local_part + carried
    scale = lax.rsqrt(jnp.mean(attended * attended, axis=2, keepdims=True) + 1e-06)
    normed = (attended * scale).reshape(tok_count, width_local).astype(BF16)

    w_other = swap_cores(w_output)
    quarter = w_output.shape[1] // 2
    n = 4
    h = lax.axis_index("head")

    halves = jnp.stack([w_output, w_other])
    pieces = []
    for o in range(n):
        q = (h + o) % n
        k = jnp.where(q // 2 == c, 0, 1)
        piece = lax.dynamic_slice(halves, (k, 0, (q % 2) * quarter), (1, halves.shape[1], quarter))
        pieces.append(piece[0])
    early = jnp.dot(normed, jnp.concatenate([pieces[3], pieces[1]], axis=1), preferred_element_type=F32)
    late = jnp.dot(normed, jnp.concatenate([pieces[2], pieces[0]], axis=1), preferred_element_type=F32)
    where_is = {3: (early, 0), 1: (early, 1), 2: (late, 0), 0: (late, 1)}

    def block(o):
        held, k = where_is[o]
        return held[:, k * quarter : (k + 1) * quarter]

    right = jnp.zeros((tok_count, quarter), F32)
    left = jnp.zeros((tok_count, quarter), F32)
    for s in range(1, n):
        send_r = (block(n - s) + right).astype(BF16)
        send_l = (block(s) + left).astype(BF16)
        send_r, send_l = lax.optimization_barrier((send_r, send_l))
        rpairs = [(j, j + 1) for j in range(s) if j + 1 < n]
        lpairs = [(j, j - 1) for j in range(n - s, n) if j - 1 >= 0]
        if s == 1:
            got = lax.ppermute(jnp.where(h == 0, send_r, send_l), "head", rpairs + lpairs).astype(F32)
            right = jnp.where(h == 1, got, 0.0)
            left = jnp.where(h == n - 2, got, 0.0)
            continue
        right = lax.ppermute(send_r, "head", rpairs).astype(F32)
        left = lax.ppermute(send_l, "head", lpairs).astype(F32)
    mixed = (block(0) + right + left).astype(BF16)
    return mixed.reshape(1, tok_count, quarter)


def solution(mesh):
    import functools

    placed = (
        P("wt", "seq", None),
        P("wt", "head"),
        P("wt", "head"),
        P("wt", "head"),
        P("head", "wt"),
    )
    return jax.shard_map(
        functools.partial(shards, mesh.shape["seq"]),
        mesh=mesh,
        in_specs=placed,
        out_specs=P("wt", "seq", "head"),
        check_vma=False,
    )
```

```python
import jax
import jax.numpy as jnp
from jax import lax
from jax.sharding import PartitionSpec as P

HD = 128
F32 = jnp.float32
BF16 = jnp.bfloat16


def swap_cores(x):
    return lax.ppermute(x, "wt", [(0, 1), (1, 0)])


def shifted(x, axis, pairs):
    return lax.ppermute(x, axis, pairs)


def prefix_over_seq(state, seq_size):
    nx, ny = 4, 4
    nz = seq_size // (nx * ny)
    i = lax.axis_index("seq")
    x = i % nx
    y = (i // nx) % ny

    def along(value, stride, size, pos):
        sent = value.astype(BF16)
        before = jnp.zeros_like(value)
        total = value
        for d in range(1, size):
            pairs = []
            for j in range(seq_size):
                jp = (j // stride) % size
                pairs.append((j, j + (((jp + d) % size) - jp) * stride))
            got = shifted(sent, "seq", pairs).astype(F32)
            before = before + jnp.where((pos - d) % size < pos, got, 0.0)
            total = total + got
        return before, total

    ex, row_total = along(state, 1, nx, x)
    ey, plane_total = along(row_total, nx, ny, y)
    ez = jnp.zeros_like(state)
    if nz > 1:
        plane = nx * ny
        zpairs = [(j, j + plane) for j in range(seq_size - plane)]
        ez = shifted(plane_total.astype(BF16), "seq", zpairs).astype(F32)
    return ex + ey + ez


def shards(seq_size, tokens, w_query, w_key, w_value, w_output):
    rows_in = tokens.reshape(tokens.shape[1], tokens.shape[2])
    tok_count = rows_in.shape[0]
    half = w_query.shape[0]
    width_local = w_query.shape[1]
    head_count = width_local // HD
    c = lax.axis_index("wt")

    mine_cols = lax.dynamic_slice_in_dim(rows_in, c * half, half, axis=1)
    got_cols = lax.dynamic_slice_in_dim(swap_cores(rows_in), c * half, half, axis=1)
    sums = []
    for w in (w_query, w_key, w_value):
        lent = swap_cores(jnp.dot(got_cols, w, preferred_element_type=F32))
        own = jnp.dot(mine_cols, w, preferred_element_type=F32)
        sums.append(own + lent)
    query_sum, key_sum, value_sum = sums

    queries = jax.nn.silu(query_sum).astype(BF16).reshape(tok_count, head_count, HD)
    keys_all = jax.nn.silu(key_sum).astype(BF16).reshape(tok_count, head_count, HD)
    values = value_sum.astype(BF16).reshape(tok_count, head_count, HD)
    local_state = jnp.einsum("thd,the->hde", keys_all, values, preferred_element_type=F32)
    prefix_state = prefix_over_seq(local_state, seq_size)

    scores = jnp.einsum("thd,shd->hts", queries, keys_all, preferred_element_type=F32)
    positions = jnp.arange(tok_count)
    causal = (positions[None, :] <= positions[:, None]).astype(F32)
    scores = (scores * causal[None, :, :]).astype(BF16)
    local_part = jnp.einsum("hts,shd->thd", scores, values, preferred_element_type=F32)
    carried = jnp.einsum(
        "thd,hde->the", queries.astype(F32), prefix_state.astype(BF16).astype(F32), preferred_element_type=F32
    )
    attended = local_part + carried
    scale = lax.rsqrt(jnp.mean(attended * attended, axis=2, keepdims=True) + 1e-06)
    normed = (attended * scale).reshape(tok_count, width_local).astype(BF16)

    w_other = swap_cores(w_output)
    quarter = w_output.shape[1] // 2
    n = 4
    h = lax.axis_index("head")

    halves = jnp.stack([w_output, w_other])
    pieces = []
    for o in range(n):
        q = (h + o) % n
        k = jnp.where(q // 2 == c, 0, 1)
        piece = lax.dynamic_slice(halves, (k, 0, (q % 2) * quarter), (1, halves.shape[1], quarter))
        pieces.append(piece[0])
    early = jnp.dot(normed, jnp.concatenate([pieces[3], pieces[1]], axis=1), preferred_element_type=F32)
    late = jnp.dot(normed, jnp.concatenate([pieces[2], pieces[0]], axis=1), preferred_element_type=F32)
    where_is = {3: (early, 0), 1: (early, 1), 2: (late, 0), 0: (late, 1)}

    def block(o):
        held, k = where_is[o]
        return held[:, k * quarter : (k + 1) * quarter]

    right = jnp.zeros((tok_count, quarter), F32)
    left = jnp.zeros((tok_count, quarter), F32)
    for s in range(1, n):
        send_r = (block(n - s) + right).astype(BF16)
        send_l = (block(s) + left).astype(BF16)
        send_r, send_l = lax.optimization_barrier((send_r, send_l))
        rpairs = [(j, j + 1) for j in range(s) if j + 1 < n]
        lpairs = [(j, j - 1) for j in range(n - s, n) if j - 1 >= 0]
        if s == 1:
            got = lax.ppermute(jnp.where(h == 0, send_r, send_l), "head", rpairs + lpairs).astype(F32)
            right = jnp.where(h == 1, got, 0.0)
            left = jnp.where(h == n - 2, got, 0.0)
            continue
        right = lax.ppermute(send_r, "head", rpairs).astype(F32)
        left = lax.ppermute(send_l, "head", lpairs).astype(F32)
    mixed = (block(0) + right + left).astype(BF16)
    return mixed.reshape(1, tok_count, quarter)


def solution(mesh):
    import functools

    placed = (
        P("wt", "seq", None),
        P("wt", "head"),
        P("wt", "head"),
        P("wt", "head"),
        P("head", "wt"),
    )
    return jax.shard_map(
        functools.partial(shards, mesh.shape["seq"]),
        mesh=mesh,
        in_specs=placed,
        out_specs=P("wt", "seq", "head"),
        check_vma=False,
    )
```

```python
import jax
import jax.numpy as jnp
from jax import lax
from jax.sharding import PartitionSpec as P

HD = 128
F32 = jnp.float32
BF16 = jnp.bfloat16


def swap_cores(x):
    return lax.ppermute(x, "wt", [(0, 1), (1, 0)])


def shifted(x, axis, pairs):
    return lax.ppermute(x, axis, pairs)


def prefix_over_seq(state, seq_size):
    nx, ny = 4, 4
    nz = seq_size // (nx * ny)
    i = lax.axis_index("seq")
    x = i % nx
    y = (i // nx) % ny

    def along(value, stride, size, pos):
        sent = value.astype(BF16)
        before = jnp.zeros_like(value)
        total = value
        for d in range(1, size):
            pairs = []
            for j in range(seq_size):
                jp = (j // stride) % size
                pairs.append((j, j + (((jp + d) % size) - jp) * stride))
            got = shifted(sent, "seq", pairs).astype(F32)
            before = before + jnp.where((pos - d) % size < pos, got, 0.0)
            total = total + got
        return before, total

    ex, row_total = along(state, 1, nx, x)
    ey, plane_total = along(row_total, nx, ny, y)
    ez = jnp.zeros_like(state)
    if nz > 1:
        plane = nx * ny
        zpairs = [(j, j + plane) for j in range(seq_size - plane)]
        ez = shifted(plane_total.astype(BF16), "seq", zpairs).astype(F32)
    return ex + ey + ez


def shards(seq_size, tokens, w_query, w_key, w_value, w_output):
    rows_in = tokens.reshape(tokens.shape[1], tokens.shape[2])
    tok_count = rows_in.shape[0]
    half = w_query.shape[0]
    width_local = w_query.shape[1]
    head_count = width_local // HD
    c = lax.axis_index("wt")

    mine_cols = lax.dynamic_slice_in_dim(rows_in, c * half, half, axis=1)
    got_cols = lax.dynamic_slice_in_dim(swap_cores(rows_in), c * half, half, axis=1)
    sums = []
    for w in (w_query, w_key, w_value):
        lent = swap_cores(jnp.dot(got_cols, w, preferred_element_type=F32))
        own = jnp.dot(mine_cols, w, preferred_element_type=F32)
        sums.append(own + lent)
    query_sum, key_sum, value_sum = sums

    queries = jax.nn.silu(query_sum).astype(BF16).reshape(tok_count, head_count, HD)
    keys_all = jax.nn.silu(key_sum).astype(BF16).reshape(tok_count, head_count, HD)
    values = value_sum.astype(BF16).reshape(tok_count, head_count, HD)
    local_state = jnp.einsum("thd,the->hde", keys_all, values, preferred_element_type=F32)
    prefix_state = prefix_over_seq(local_state, seq_size)

    scores = jnp.einsum("thd,shd->hts", queries, keys_all, preferred_element_type=F32)
    positions = jnp.arange(tok_count)
    causal = (positions[None, :] <= positions[:, None]).astype(F32)
    scores = (scores * causal[None, :, :]).astype(BF16)
    local_part = jnp.einsum("hts,shd->thd", scores, values, preferred_element_type=F32)
    carried = jnp.einsum(
        "thd,hde->the", queries.astype(F32), prefix_state.astype(BF16).astype(F32), preferred_element_type=F32
    )
    attended = local_part + carried
    scale = lax.rsqrt(jnp.mean(attended * attended, axis=2, keepdims=True) + 1e-06)
    normed = (attended * scale).reshape(tok_count, width_local).astype(BF16)

    w_late, _ = lax.optimization_barrier((w_output, value_sum))
    w_other = swap_cores(w_late)
    quarter = w_output.shape[1] // 2
    n = 4
    h = lax.axis_index("head")

    halves = jnp.stack([w_output, w_other])
    pieces = []
    for o in range(n):
        q = (h + o) % n
        k = jnp.where(q // 2 == c, 0, 1)
        piece = lax.dynamic_slice(halves, (k, 0, (q % 2) * quarter), (1, halves.shape[1], quarter))
        pieces.append(piece[0])
    rotated = jnp.concatenate(pieces, axis=1)
    products = jnp.dot(normed, rotated, preferred_element_type=F32)

    def block(o):
        return products[:, o * quarter : (o + 1) * quarter]

    right = jnp.zeros((tok_count, quarter), F32)
    left = jnp.zeros((tok_count, quarter), F32)
    for s in range(1, n):
        send_r = (block(n - s) + right).astype(BF16)
        send_l = (block(s) + left).astype(BF16)
        send_r, send_l = lax.optimization_barrier((send_r, send_l))
        rpairs = [(j, j + 1) for j in range(s) if j + 1 < n]
        lpairs = [(j, j - 1) for j in range(n - s, n) if j - 1 >= 0]
        right = lax.ppermute(send_r, "head", rpairs).astype(F32)
        left = lax.ppermute(send_l, "head", lpairs).astype(F32)
    mixed = (block(0) + right + left).astype(BF16)
    return mixed.reshape(1, tok_count, quarter)


def solution(mesh):
    import functools

    placed = (
        P("wt", "seq", None),
        P("wt", "head"),
        P("wt", "head"),
        P("wt", "head"),
        P("head", "wt"),
    )
    return jax.shard_map(
        functools.partial(shards, mesh.shape["seq"]),
        mesh=mesh,
        in_specs=placed,
        out_specs=P("wt", "seq", "head"),
        check_vma=False,
    )
```

```python
import jax
import jax.numpy as jnp
from jax import lax
from jax.sharding import PartitionSpec as P

HD = 128
F32 = jnp.float32
BF16 = jnp.bfloat16


def swap_cores(x):
    return lax.ppermute(x, "wt", [(0, 1), (1, 0)])


def shifted(x, axis, pairs):
    return lax.ppermute(x, axis, pairs)


def prefix_over_seq(state, seq_size):
    nx, ny = 4, 4
    nz = seq_size // (nx * ny)
    i = lax.axis_index("seq")
    x = i % nx
    y = (i // nx) % ny

    def along(value, stride, size, pos):
        sent = value.astype(BF16)
        before = jnp.zeros_like(value)
        total = value
        for d in sorted(range(1, size), key=lambda d: -min(d, size - d)):
            pairs = []
            for j in range(seq_size):
                jp = (j // stride) % size
                pairs.append((j, j + (((jp + d) % size) - jp) * stride))
            got = shifted(sent, "seq", pairs).astype(F32)
            before = before + jnp.where((pos - d) % size < pos, got, 0.0)
            total = total + got
        return before, total

    ex, row_total = along(state, 1, nx, x)
    ey, plane_total = along(row_total, nx, ny, y)
    ez = jnp.zeros_like(state)
    if nz > 1:
        plane = nx * ny
        zpairs = [(j, j + plane) for j in range(seq_size - plane)]
        ez = shifted(plane_total.astype(BF16), "seq", zpairs).astype(F32)
    return ex + ey + ez


def shards(seq_size, tokens, w_query, w_key, w_value, w_output):
    rows_in = tokens.reshape(tokens.shape[1], tokens.shape[2])
    tok_count = rows_in.shape[0]
    half = w_query.shape[0]
    width_local = w_query.shape[1]
    head_count = width_local // HD
    c = lax.axis_index("wt")

    mine_cols = lax.dynamic_slice_in_dim(rows_in, c * half, half, axis=1)
    got_cols = lax.dynamic_slice_in_dim(swap_cores(rows_in), c * half, half, axis=1)
    sums = []
    for w in (w_query, w_key, w_value):
        lent = swap_cores(jnp.dot(got_cols, w, preferred_element_type=F32))
        own = jnp.dot(mine_cols, w, preferred_element_type=F32)
        sums.append(own + lent)
    query_sum, key_sum, value_sum = sums

    queries = jax.nn.silu(query_sum).astype(BF16).reshape(tok_count, head_count, HD)
    keys_all = jax.nn.silu(key_sum).astype(BF16).reshape(tok_count, head_count, HD)
    values = value_sum.astype(BF16).reshape(tok_count, head_count, HD)
    local_state = jnp.einsum("thd,the->hde", keys_all, values, preferred_element_type=F32)
    prefix_state = prefix_over_seq(local_state, seq_size)

    scores = jnp.einsum("thd,shd->hts", queries, keys_all, preferred_element_type=F32)
    positions = jnp.arange(tok_count)
    causal = (positions[None, :] <= positions[:, None]).astype(F32)
    scores = (scores * causal[None, :, :]).astype(BF16)
    local_part = jnp.einsum("hts,shd->thd", scores, values, preferred_element_type=F32)
    carried = jnp.einsum(
        "thd,hde->the", queries.astype(F32), prefix_state.astype(BF16).astype(F32), preferred_element_type=F32
    )
    attended = local_part + carried
    scale = lax.rsqrt(jnp.mean(attended * attended, axis=2, keepdims=True) + 1e-06)
    normed = (attended * scale).reshape(tok_count, width_local).astype(BF16)

    w_other = swap_cores(w_output)
    quarter = w_output.shape[1] // 2
    n = 4
    h = lax.axis_index("head")

    halves = jnp.stack([w_output, w_other])
    pieces = []
    for o in range(n):
        q = (h + o) % n
        k = jnp.where(q // 2 == c, 0, 1)
        piece = lax.dynamic_slice(halves, (k, 0, (q % 2) * quarter), (1, halves.shape[1], quarter))
        pieces.append(piece[0])
    rotated = jnp.concatenate(pieces, axis=1)
    products = jnp.dot(normed, rotated, preferred_element_type=F32)

    def block(o):
        return products[:, o * quarter : (o + 1) * quarter]

    right = jnp.zeros((tok_count, quarter), F32)
    left = jnp.zeros((tok_count, quarter), F32)
    for s in range(1, n):
        send_r = (block(n - s) + right).astype(BF16)
        send_l = (block(s) + left).astype(BF16)
        send_r, send_l = lax.optimization_barrier((send_r, send_l))
        rpairs = [(j, j + 1) for j in range(s) if j + 1 < n]
        lpairs = [(j, j - 1) for j in range(n - s, n) if j - 1 >= 0]
        right = lax.ppermute(send_r, "head", rpairs).astype(F32)
        left = lax.ppermute(send_l, "head", lpairs).astype(F32)
    mixed = (block(0) + right + left).astype(BF16)
    return mixed.reshape(1, tok_count, quarter)


def solution(mesh):
    import functools

    placed = (
        P("wt", "seq", None),
        P("wt", "head"),
        P("wt", "head"),
        P("wt", "head"),
        P("head", "wt"),
    )
    return jax.shard_map(
        functools.partial(shards, mesh.shape["seq"]),
        mesh=mesh,
        in_specs=placed,
        out_specs=P("wt", "seq", "head"),
        check_vma=False,
    )
```
